512 devices in a mesh: dp: 8 (over x, y_hi), expert: 64 (over y_lo, z, core).
Axes of the slice: x: 4, y: 4 (y_hi: 2, y_lo: 2; y = y_hi * 2 + y_lo), z: 16, core: 2. Of those that a mesh axis runs over, the one named last changes fastest.
Arguments:
- tokens: bfloat16 [65536, 2048], P(('dp', 'expert')), may hold values from -6 to 6
- out_grad: bfloat16 [65536, 2048], P(('dp', 'expert')), may hold values from -6 to 6
- combine: float32 [65536, 2], P(('dp', 'expert')), may hold values from 0.1 to 1
- expert_ids: int32 [65536, 2], P(('dp', 'expert')), may hold values from 0 to 63, all different within a row; in each aligned block of 128 rows (0 to 127, 128 to 255, ...) at most 5 rows name the same one
- gate_weight: bfloat16 [64, 2048, 768], P('expert', 'dp'), may hold values from -0.125 to 0.125
- up_weight: bfloat16 [64, 2048, 768], P('expert', 'dp'), may hold values from -0.125 to 0.125
- down_weight: bfloat16 [64, 2048, 768], P('expert', 'dp'), may hold values from -0.21875 to 0.21875
Outputs:
- token_grad: bfloat16 [65536, 2048], P(('dp', 'expert'))
- down_grad: bfloat16 [64, 2048, 768], P('expert', 'dp')
The draws below stay inside these ranges and needn't reach their ends.
Inputs may be any that keep to these rules, and one draw needn't show every extreme that they name: `expert_ids`: each row names 2 different experts. Among the 128 rows of one device no expert is named more than 5 times, a bound that some block reaches.
All inputs are finite; a program needn't handle non-finite values.
Results may differ from the reference program's by a relative error of at most 0.012.
Values may be sent and summed in bfloat16 or wider, within the bound.
No kernel may reach another device: no remote copies, remote signals or barrier semaphores. Data moves between devices by JAX's collectives and lax.ppermute only.
A program may use at most 64 MiB of HBM per device.

```python
import math
import jax
import jax.numpy as jnp
import numpy as np
from jax import lax

D = 2048
FF = 768
TOP = 2
TOK_DEV = 128
EXPERTS = 64
CAP = 5
TOKENS = 65536
N_DP = 8
N_EXPERT = 64


def shard_levels(key, dims, pieces, least, top_value):
    loudness, own = 1.0, jax.random.fold_in(key, 6)
    for position, shards_of in pieces:
        steps = jnp.exp(jax.random.uniform(jax.random.fold_in(own, position), (shards_of,), jnp.float32, least / len(pieces), top_value / len(pieces)))
        loudness = loudness * jnp.repeat(steps, dims[position] // shards_of).reshape([-1 if axis == position else 1 for axis in range(len(dims))])
    return loudness


def shared_out(rng, own, number, rows, amount, top, reach, slope):
    sequence = jax.random.permutation(rng, amount)
    heavy_load, ordinary = shares(amount, rows * top, reach, slope, True), shares(amount, rows * top, reach, slope, False)
    places = jnp.arange(amount)

    def named(tallies, rotation):
        used = int((tallies > 0).sum())
        fixed = max(1, used // 4)
        moved = fixed + (places - fixed + rotation * (used - fixed)) % max(1, amount - fixed)
        return jnp.zeros((amount,), jnp.int32).at[sequence[jnp.where(places < fixed, places, moved)]].set(jnp.asarray(tallies, jnp.int32))

    tallies = jnp.where(number % 4 == 0, named(heavy_load, number // 4), named(ordinary, number - number // 4 - 1))
    mixed = jax.random.permutation(jax.random.fold_in(own, 3), amount)
    donor, sink = mixed[0:amount // 2 * 2:2], mixed[1:amount // 2 * 2:2]
    slack = jnp.minimum(tallies[donor] - 1, reach - tallies[sink]) // 2
    slack = jnp.where((donor == sequence[0]) | (sink == sequence[0]) | (tallies[sink] == 0), 0, jnp.maximum(slack, 0))
    moved = jax.random.randint(jax.random.fold_in(own, 4), (amount // 2,), 0, 1 << 20) % (slack + 1)
    tallies = tallies.at[donor].add(-moved).at[sink].add(moved)
    labels = jnp.searchsorted(jnp.cumsum(tallies), jnp.arange(rows * top), side="right").astype(jnp.int32)
    table = labels.reshape(top, rows).T
    table = table[jax.random.permutation(jax.random.fold_in(own, 1), rows)]
    rotation = jax.random.randint(jax.random.fold_in(own, 2), (rows, 1), 0, top)
    return jnp.take_along_axis(table, (jnp.arange(top)[None, :] + rotation) % top, axis=1)


def shares(count, total, most, skew, full):
    loads = [(1 << 20) // math.isqrt(rank ** skew) + 1 for rank in range(1, count + 1)]
    largest = most if full else min(most, max(-(-total // count), total * loads[0] // sum(loads)))
    least = 1 if total - largest >= count - 1 else 0
    holding, spare = [largest] + [least] * (count - 1), total - largest - least * (count - 1)
    while spare > 0:
        free = [i for i in range(1, count) if holding[i] < largest] or [i for i in range(1, count) if holding[i] < most]
        whole, budget = sum([loads[i] for i in free]), spare
        for i in free:
            more = min(most - holding[i], max(1, budget * loads[i] // whole), spare)
            holding[i] = holding[i] + more
            spare = spare - more
    return np.array(holding)


def centred(rng, dims, spread, bound, shards=(), kind=jnp.bfloat16):
    drawn = spread * jax.random.normal(rng, dims, jnp.float32)
    if shards:
        drawn = drawn * shard_levels(rng, dims, shards, -0.22, 0.18)
    return jnp.clip(drawn, -bound, bound).astype(kind)


def setup_inputs(seed: int = 0) -> dict:
    key_of = jax.random.split(jax.random.key(seed), 8)
    tokens = centred(key_of[0], (TOKENS, D), 1.0, 6.0, ((0, 512),))
    out_grad = centred(key_of[1], (TOKENS, D), 1.0, 6.0, ((0, 512),))
    combine = jnp.clip(jnp.exp(math.log(1.0) - 2.3025851 * jax.random.uniform(key_of[2], (TOKENS, TOP), jnp.float32) ** shard_levels(key_of[2], (TOKENS, TOP), ((0, 512),), -0.2, 0.2)), 0.1, 1.0)
    expert_ids_keys = jax.random.split(jax.random.fold_in(key_of[3], 1), TOKENS // TOK_DEV)
    expert_ids_turns = jax.random.permutation(jax.random.fold_in(key_of[3], 3), TOKENS // TOK_DEV)
    expert_ids = jax.vmap(lambda own, number: shared_out(jax.random.fold_in(key_of[3], 2), own, number, TOK_DEV, EXPERTS, TOP, CAP, 2))(expert_ids_keys, expert_ids_turns).reshape((TOKENS, TOP))
    gate_weight = centred(key_of[4], (EXPERTS, D, FF), D ** -0.5, 0.125, ((0, 64), (1, 8)))
    up_weight = centred(key_of[5], (EXPERTS, D, FF), D ** -0.5, 0.125, ((0, 64), (1, 8)))
    down_weight = centred(key_of[6], (EXPERTS, D, FF), FF ** -0.5, 0.21875, ((0, 64), (1, 8)))
    return {"tokens": tokens, "out_grad": out_grad, "combine": combine, "expert_ids": expert_ids, "gate_weight": gate_weight, "up_weight": up_weight, "down_weight": down_weight}


def reference(tokens, out_grad, combine, expert_ids, gate_weight, up_weight, down_weight):
    blocks = N_DP * N_EXPERT
    pairs = TOK_DEV * TOP
    block_ids = expert_ids.reshape(blocks, pairs)
    onehot = (block_ids[:, :, None] == jnp.arange(EXPERTS, dtype=jnp.int32)[None, None, :]).astype(jnp.int32)
    earlier = jnp.cumsum(onehot, axis=1) - onehot
    slot_index = jnp.sum(earlier * onehot, axis=2).astype(jnp.int32)
    block_index = jnp.broadcast_to(jnp.arange(blocks, dtype=jnp.int32)[:, None], (blocks, pairs))
    dp_index = block_index // N_EXPERT
    source_index = block_index % N_EXPERT
    assigned = jnp.arange(blocks * pairs, dtype=jnp.int32).reshape(blocks, pairs)
    slot_lookup_table = jnp.full((N_DP, EXPERTS, N_EXPERT, CAP), -1, dtype=jnp.int32)
    slot_lookup_table = slot_lookup_table.at[dp_index, block_ids, source_index, slot_index].set(assigned)
    slot_lookup_table = jnp.transpose(slot_lookup_table, (1, 0, 2, 3)).reshape(EXPERTS, N_DP * N_EXPERT * CAP)
    combine_flat = combine.reshape(-1)

    def per_expert(accumulated, inputs):
        row_ids, w_gate, w_up, w_down = inputs
        is_valid = row_ids >= 0
        safe_index = jnp.where(is_valid, row_ids, 0)
        token_index = (safe_index // TOP).astype(jnp.int32)
        rows = jnp.where(is_valid[:, None], tokens[token_index], jnp.zeros((), jnp.bfloat16)).astype(jnp.bfloat16)
        weight_row = jnp.where(is_valid, combine_flat[safe_index], jnp.float32(0.0))
        grads = (weight_row[:, None] * out_grad[token_index].astype(jnp.float32)).astype(jnp.bfloat16)
        gate_pre = jnp.dot(rows, w_gate, preferred_element_type=jnp.float32)
        up_pre = jnp.dot(rows, w_up, preferred_element_type=jnp.float32)
        sigmoid_gate = jax.nn.sigmoid(gate_pre)
        silu_gate = gate_pre * sigmoid_gate
        hidden = (silu_gate * up_pre).astype(jnp.bfloat16)
        hidden_grad = jnp.dot(grads, w_down, preferred_element_type=jnp.float32)
        gate_grad = (hidden_grad * up_pre * sigmoid_gate * (1.0 + gate_pre * (1.0 - sigmoid_gate))).astype(jnp.bfloat16)
        up_grad = (hidden_grad * silu_gate).astype(jnp.bfloat16)
        row_grad = (jnp.dot(gate_grad, w_gate.T, preferred_element_type=jnp.float32)
                    + jnp.dot(up_grad, w_up.T, preferred_element_type=jnp.float32)).astype(jnp.bfloat16)
        accumulated = accumulated.at[token_index].add(
            jnp.where(is_valid[:, None], row_grad.astype(jnp.float32), jnp.float32(0.0)))
        gradient_pieces = grads.reshape(N_DP, N_EXPERT * CAP, D).astype(jnp.float32)
        hidden_pieces = hidden.reshape(N_DP, N_EXPERT * CAP, FF).astype(jnp.float32)
        down_contribution = jnp.einsum("czm,czp->cmp", gradient_pieces, hidden_pieces,
                               precision=lax.Precision.HIGHEST).astype(jnp.bfloat16)
        down_contribution = lax.optimization_barrier(down_contribution)
        down_grad = jnp.sum(down_contribution.astype(jnp.float32), axis=0).astype(jnp.bfloat16)
        return accumulated, down_grad

    start_sum = jnp.zeros((TOKENS, D), jnp.float32)
    total_grad, down_grad = lax.scan(per_expert, start_sum, (slot_lookup_table, gate_weight, up_weight, down_weight))
    return total_grad.astype(jnp.bfloat16), down_grad
```

```python
import jax
import jax.numpy as jnp
from jax import lax
from jax.sharding import Mesh
from jax.sharding import PartitionSpec as P

TOP = 2
CAP = 5
SUB = ("ylo", "z", "core")
ROWS = ("dp",) + SUB


def local_then_z(x, kinds):
    x = lax.all_to_all(x, "core", 3, 3, tiled=True)
    x = lax.all_to_all(x, "ylo", 1, 1, tiled=True)
    return [lax.all_to_all(x[k], "z", 1, 1, tiled=True) for k in range(kinds)]


def z_then_local(x):
    x = lax.all_to_all(x, "z", 1, 1, tiled=True)
    x = lax.all_to_all(x, "ylo", 0, 0, tiled=True)
    return lax.all_to_all(x, "core", 2, 2, tiled=True)


def body(tokens, out_grad, combine, expert_ids, gate_weight, up_weight, down_weight):
    token_rows = tokens.shape[0]
    width = tokens.shape[1]
    n_ylo, n_z, n_core = (lax.axis_size(a) for a in SUB)
    expert_count = n_ylo * n_z * n_core
    capacity = CAP
    positions = expert_count * capacity
    w_gate = lax.all_gather(gate_weight, "dp", axis=1, tiled=True)[0]
    w_up = lax.all_gather(up_weight, "dp", axis=1, tiled=True)[0]
    w_down = lax.all_gather(down_weight, "dp", axis=1, tiled=True)[0]
    flat_ids = expert_ids.reshape(-1)
    onehot = (flat_ids[:, None] == jnp.arange(expert_count, dtype=jnp.int32)[None, :]).astype(jnp.int32)
    earlier = jnp.cumsum(onehot, axis=0) - onehot
    slot_index = jnp.sum(earlier * onehot, axis=1)
    target = flat_ids * capacity + slot_index
    matches = target[None, :] == jnp.arange(positions, dtype=jnp.int32)[:, None]
    picker = jnp.sum(
        matches.reshape(positions, token_rows, TOP).astype(jnp.float32), axis=2
    ).astype(jnp.bfloat16)
    slot_weight = jnp.sum(jnp.where(matches, combine.reshape(-1)[None, :], jnp.float32(0.0)), axis=1)
    row_send = jnp.dot(picker, tokens, preferred_element_type=jnp.float32).astype(jnp.bfloat16)
    picked_grad = jnp.dot(picker, out_grad, preferred_element_type=jnp.float32)
    grad_send = (slot_weight[:, None] * picked_grad).astype(jnp.bfloat16)
    send = jnp.stack([row_send, grad_send]).reshape(2, n_ylo, n_z, n_core, capacity, width)
    rows_in, grads_in = local_then_z(send, 2)
    rows_in = rows_in.reshape(positions, width)
    grads_in = grads_in.reshape(positions, width)
    gate_pre = jnp.dot(rows_in, w_gate, preferred_element_type=jnp.float32)
    up_pre = jnp.dot(rows_in, w_up, preferred_element_type=jnp.float32)
    sigmoid_gate = jax.nn.sigmoid(gate_pre)
    silu_gate = gate_pre * sigmoid_gate
    hidden = (silu_gate * up_pre).astype(jnp.bfloat16)
    hidden_grad = jnp.dot(grads_in, w_down, preferred_element_type=jnp.float32)
    gate_grad = (
        hidden_grad * up_pre * sigmoid_gate * (1.0 + gate_pre * (1.0 - sigmoid_gate))
    ).astype(jnp.bfloat16)
    up_grad = (hidden_grad * silu_gate).astype(jnp.bfloat16)
    contract_hidden = (((1,), (1,)), ((), ()))
    row_grad = (
        lax.dot_general(gate_grad, w_gate, contract_hidden, preferred_element_type=jnp.float32)
        + lax.dot_general(up_grad, w_up, contract_hidden, preferred_element_type=jnp.float32)
    ).astype(jnp.bfloat16)
    back_rows = z_then_local(row_grad.reshape(n_ylo, n_z, n_core, capacity, width))
    token_grad = lax.dot_general(
        picker,
        back_rows.reshape(positions, width),
        (((0,), (0,)), ((), ())),
        preferred_element_type=jnp.float32,
    ).astype(jnp.bfloat16)
    down_grad = lax.psum_scatter(
        lax.dot_general(
            grads_in, hidden, (((0,), (0,)), ((), ())), preferred_element_type=jnp.float32
        ).astype(jnp.bfloat16),
        "dp",
        scatter_dimension=0,
        tiled=True,
    )
    return (token_grad, down_grad[None])


def solution(mesh):
    n_dp, n_expert = mesh.devices.shape
    fine = Mesh(mesh.devices.reshape(n_dp, 2, n_expert // 4, 2), ("dp",) + SUB)
    rows = P(ROWS, None)
    weights = P(SUB, "dp", None)
    return jax.shard_map(
        body,
        mesh=fine,
        in_specs=(rows, rows, rows, rows, weights, weights, weights),
        out_specs=(rows, weights),
        check_vma=False,
    )
```

```python
import jax
import jax.numpy as jnp
from jax import lax
from jax.sharding import Mesh
from jax.sharding import PartitionSpec as P

TOP = 2
CAP = 5
SUB = ("ylo", "z", "core")
ROWS = ("dp",) + SUB
SWAP = [(0, 1), (1, 0)]


def swap_half(x, axis_name, dim):
    stay = lax.index_in_dim(x, 0, dim, keepdims=True)
    go = lax.index_in_dim(x, 1, dim, keepdims=True)
    got = lax.ppermute(go, axis_name, SWAP)
    return jnp.concatenate([stay, got], dim)


def forward_move(x):
    x = swap_half(x, "core", 0)
    x = swap_half(x, "ylo", 1)
    return lax.all_to_all(x, "z", 2, 2, tiled=True)


def backward_move(x):
    x = lax.all_to_all(x, "z", 2, 2, tiled=True)
    x = swap_half(x, "ylo", 1)
    return swap_half(x, "core", 0)


def body(tokens, out_grad, combine, expert_ids, gate_weight, up_weight, down_weight):
    token_rows = tokens.shape[0]
    width = tokens.shape[1]
    n_ylo, n_z, n_core = (lax.axis_size(a) for a in SUB)
    expert_count = n_ylo * n_z * n_core
    capacity = CAP
    positions = expert_count * capacity
    stacked = lax.all_gather(
        jnp.concatenate([gate_weight, up_weight, down_weight], 0), "dp", axis=1, tiled=True
    )
    w_gate, w_up, w_down = stacked[0], stacked[1], stacked[2]
    flat_ids = expert_ids.reshape(-1)
    onehot = (flat_ids[:, None] == jnp.arange(expert_count, dtype=jnp.int32)[None, :]).astype(jnp.int32)
    earlier = jnp.cumsum(onehot, axis=0) - onehot
    slot_index = jnp.sum(earlier * onehot, axis=1)
    my_core = lax.axis_index("core")
    my_ylo = lax.axis_index("ylo")
    e_core = flat_ids % n_core
    e_z = (flat_ids // n_core) % n_z
    e_ylo = flat_ids // (n_core * n_z)
    rel = ((e_core ^ my_core) * n_ylo + (e_ylo ^ my_ylo)) * n_z + e_z
    target = rel * capacity + slot_index
    matches = target[None, :] == jnp.arange(positions, dtype=jnp.int32)[:, None]
    picker = jnp.sum(
        matches.reshape(positions, token_rows, TOP).astype(jnp.float32), axis=2
    ).astype(jnp.bfloat16)
    slot_weight = jnp.sum(jnp.where(matches, combine.reshape(-1)[None, :], jnp.float32(0.0)), axis=1)
    row_send = jnp.dot(picker, tokens, preferred_element_type=jnp.float32).astype(jnp.bfloat16)
    picked_grad = jnp.dot(picker, out_grad, preferred_element_type=jnp.float32)
    grad_send = (slot_weight[:, None] * picked_grad).astype(jnp.bfloat16)
    block = (n_core, n_ylo, n_z, capacity, width)
    rows_in = forward_move(row_send.reshape(block)).reshape(positions, width)
    grads_in = forward_move(grad_send.reshape(block)).reshape(positions, width)
    gate_pre = jnp.dot(rows_in, w_gate, preferred_element_type=jnp.float32)
    up_pre = jnp.dot(rows_in, w_up, preferred_element_type=jnp.float32)
    sigmoid_gate = jax.nn.sigmoid(gate_pre)
    silu_gate = gate_pre * sigmoid_gate
    hidden = (silu_gate * up_pre).astype(jnp.bfloat16)
    hidden_grad = jnp.dot(grads_in, w_down, preferred_element_type=jnp.float32)
    gate_grad = (
        hidden_grad * up_pre * sigmoid_gate * (1.0 + gate_pre * (1.0 - sigmoid_gate))
    ).astype(jnp.bfloat16)
    up_grad = (hidden_grad * silu_gate).astype(jnp.bfloat16)
    contract_hidden = (((1,), (1,)), ((), ()))
    row_grad = (
        lax.dot_general(gate_grad, w_gate, contract_hidden, preferred_element_type=jnp.float32)
        + lax.dot_general(up_grad, w_up, contract_hidden, preferred_element_type=jnp.float32)
    ).astype(jnp.bfloat16)
    back_rows = backward_move(row_grad.reshape(block))
    token_grad = lax.dot_general(
        picker,
        back_rows.reshape(positions, width),
        (((0,), (0,)), ((), ())),
        preferred_element_type=jnp.float32,
    ).astype(jnp.bfloat16)
    down_grad = lax.psum_scatter(
        lax.dot_general(
            grads_in, hidden, (((0,), (0,)), ((), ())), preferred_element_type=jnp.float32
        ).astype(jnp.bfloat16),
        "dp",
        scatter_dimension=0,
        tiled=True,
    )
    return (token_grad, down_grad[None])


def solution(mesh):
    n_dp, n_expert = mesh.devices.shape
    fine = Mesh(mesh.devices.reshape(n_dp, 2, n_expert // 4, 2), ("dp",) + SUB)
    rows = P(ROWS, None)
    weights = P(SUB, "dp", None)
    return jax.shard_map(
        body,
        mesh=fine,
        in_specs=(rows, rows, rows, rows, weights, weights, weights),
        out_specs=(rows, weights),
        check_vma=False,
    )
```

```python
import jax
import jax.numpy as jnp
from jax import lax
from jax.sharding import Mesh
from jax.sharding import PartitionSpec as P

TOP = 2
CAP = 5
SUB = ("ylo", "z", "core")
ROWS = ("dp",) + SUB
SWAP = [(0, 1), (1, 0)]


def swap_half(x, axis_name, dim):
    stay = lax.index_in_dim(x, 0, dim, keepdims=True)
    go = lax.index_in_dim(x, 1, dim, keepdims=True)
    got = lax.ppermute(go, axis_name, SWAP)
    return jnp.concatenate([stay, got], dim)


def forward_move(x, z_first):
    if z_first:
        x = lax.all_to_all(x, "z", 2, 2, tiled=True)
    x = swap_half(x, "core", 0)
    x = swap_half(x, "ylo", 1)
    if not z_first:
        x = lax.all_to_all(x, "z", 2, 2, tiled=True)
    return x


def backward_move(x):
    x = lax.all_to_all(x, "z", 2, 2, tiled=True)
    x = swap_half(x, "ylo", 1)
    return swap_half(x, "core", 0)


def body(tokens, out_grad, combine, expert_ids, gate_weight, up_weight, down_weight):
    token_rows = tokens.shape[0]
    width = tokens.shape[1]
    n_ylo, n_z, n_core = (lax.axis_size(a) for a in SUB)
    expert_count = n_ylo * n_z * n_core
    capacity = CAP
    positions = expert_count * capacity
    stacked = lax.all_gather(
        jnp.concatenate([gate_weight, up_weight, down_weight], 0), "dp", axis=1, tiled=True
    )
    w_gate, w_up, w_down = stacked[0], stacked[1], stacked[2]
    flat_ids = expert_ids.reshape(-1)
    onehot = (flat_ids[:, None] == jnp.arange(expert_count, dtype=jnp.int32)[None, :]).astype(jnp.int32)
    earlier = jnp.cumsum(onehot, axis=0) - onehot
    slot_index = jnp.sum(earlier * onehot, axis=1)
    my_core = lax.axis_index("core")
    my_ylo = lax.axis_index("ylo")
    e_core = flat_ids % n_core
    e_z = (flat_ids // n_core) % n_z
    e_ylo = flat_ids // (n_core * n_z)
    rel = ((e_core ^ my_core) * n_ylo + (e_ylo ^ my_ylo)) * n_z + e_z
    target = rel * capacity + slot_index
    matches = target[None, :] == jnp.arange(positions, dtype=jnp.int32)[:, None]
    picker = jnp.sum(
        matches.reshape(positions, token_rows, TOP).astype(jnp.float32), axis=2
    ).astype(jnp.bfloat16)
    slot_weight = jnp.sum(jnp.where(matches, combine.reshape(-1)[None, :], jnp.float32(0.0)), axis=1)
    row_send = jnp.dot(picker, tokens, preferred_element_type=jnp.float32).astype(jnp.bfloat16)
    picked_grad = jnp.dot(picker, out_grad, preferred_element_type=jnp.float32)
    grad_send = (slot_weight[:, None] * picked_grad).astype(jnp.bfloat16)
    block = (n_core, n_ylo, n_z, capacity, width)
    rows_in = forward_move(row_send.reshape(block), True).reshape(positions, width)
    grads_in = forward_move(grad_send.reshape(block), False).reshape(positions, width)
    gate_pre = jnp.dot(rows_in, w_gate, preferred_element_type=jnp.float32)
    up_pre = jnp.dot(rows_in, w_up, preferred_element_type=jnp.float32)
    sigmoid_gate = jax.nn.sigmoid(gate_pre)
    silu_gate = gate_pre * sigmoid_gate
    hidden = (silu_gate * up_pre).astype(jnp.bfloat16)
    hidden_grad = jnp.dot(grads_in, w_down, preferred_element_type=jnp.float32)
    gate_grad = (
        hidden_grad * up_pre * sigmoid_gate * (1.0 + gate_pre * (1.0 - sigmoid_gate))
    ).astype(jnp.bfloat16)
    up_grad = (hidden_grad * silu_gate).astype(jnp.bfloat16)
    contract_hidden = (((1,), (1,)), ((), ()))
    row_grad = (
        lax.dot_general(gate_grad, w_gate, contract_hidden, preferred_element_type=jnp.float32)
        + lax.dot_general(up_grad, w_up, contract_hidden, preferred_element_type=jnp.float32)
    ).astype(jnp.bfloat16)
    back_rows = backward_move(row_grad.reshape(block))
    token_grad = lax.dot_general(
        picker,
        back_rows.reshape(positions, width),
        (((0,), (0,)), ((), ())),
        preferred_element_type=jnp.float32,
    ).astype(jnp.bfloat16)
    down_grad = lax.psum_scatter(
        lax.dot_general(
            grads_in, hidden, (((0,), (0,)), ((), ())), preferred_element_type=jnp.float32
        ).astype(jnp.bfloat16),
        "dp",
        scatter_dimension=0,
        tiled=True,
    )
    return (token_grad, down_grad[None])


def solution(mesh):
    n_dp, n_expert = mesh.devices.shape
    fine = Mesh(mesh.devices.reshape(n_dp, 2, n_expert // 4, 2), ("dp",) + SUB)
    rows = P(ROWS, None)
    weights = P(SUB, "dp", None)
    return jax.shard_map(
        body,
        mesh=fine,
        in_specs=(rows, rows, rows, rows, weights, weights, weights),
        out_specs=(rows, weights),
        check_vma=False,
    )
```

```python
import jax
import jax.numpy as jnp
from jax import lax
from jax.sharding import Mesh
from jax.sharding import PartitionSpec as P

TOP = 2
CAP = 5
SUB = ("ylo", "z", "core")
ROWS = ("dp",) + SUB
SWAP = [(0, 1), (1, 0)]


def swap_half(x, axis_name, dim):
    stay = lax.index_in_dim(x, 0, dim, keepdims=True)
    go = lax.index_in_dim(x, 1, dim, keepdims=True)
    got = lax.ppermute(go, axis_name, SWAP)
    return jnp.concatenate([stay, got], dim)


def forward_move(x, z_first):
    if z_first:
        x = lax.all_to_all(x, "z", 2, 2, tiled=True)
    x = swap_half(x, "core", 0)
    x = swap_half(x, "ylo", 1)
    if not z_first:
        x = lax.all_to_all(x, "z", 2, 2, tiled=True)
    return x


def backward_move(x, z_first):
    if z_first:
        x = lax.all_to_all(x, "z", 2, 2, tiled=True)
    x = swap_half(x, "ylo", 1)
    x = swap_half(x, "core", 0)
    if not z_first:
        x = lax.all_to_all(x, "z", 2, 2, tiled=True)
    return x


def body(tokens, out_grad, combine, expert_ids, gate_weight, up_weight, down_weight):
    token_rows = tokens.shape[0]
    width = tokens.shape[1]
    n_ylo, n_z, n_core = (lax.axis_size(a) for a in SUB)
    expert_count = n_ylo * n_z * n_core
    capacity = CAP
    positions = expert_count * capacity
    w_gate = lax.all_gather(gate_weight, "dp", axis=1, tiled=True)[0]
    w_up = lax.all_gather(up_weight, "dp", axis=1, tiled=True)[0]
    w_down = lax.all_gather(down_weight, "dp", axis=1, tiled=True)[0]
    flat_ids = expert_ids.reshape(-1)
    onehot = (flat_ids[:, None] == jnp.arange(expert_count, dtype=jnp.int32)[None, :]).astype(jnp.int32)
    earlier = jnp.cumsum(onehot, axis=0) - onehot
    slot_index = jnp.sum(earlier * onehot, axis=1)
    my_core = lax.axis_index("core")
    my_ylo = lax.axis_index("ylo")
    e_core = flat_ids % n_core
    e_z = (flat_ids // n_core) % n_z
    e_ylo = flat_ids // (n_core * n_z)
    rel = ((e_core ^ my_core) * n_ylo + (e_ylo ^ my_ylo)) * n_z + e_z
    target = rel * capacity + slot_index
    matches = target[None, :] == jnp.arange(positions, dtype=jnp.int32)[:, None]
    picker = jnp.sum(
        matches.reshape(positions, token_rows, TOP).astype(jnp.float32), axis=2
    ).astype(jnp.bfloat16)
    slot_weight = jnp.sum(jnp.where(matches, combine.reshape(-1)[None, :], jnp.float32(0.0)), axis=1)
    row_send = jnp.dot(picker, tokens, preferred_element_type=jnp.float32).astype(jnp.bfloat16)
    picked_grad = jnp.dot(picker, out_grad, preferred_element_type=jnp.float32)
    grad_send = (slot_weight[:, None] * picked_grad).astype(jnp.bfloat16)
    block = (n_core, n_ylo, n_z, capacity, width)
    rows_in = forward_move(row_send.reshape(block), True).reshape(positions, width)
    grads_in = forward_move(grad_send.reshape(block), False).reshape(positions, width)
    gate_pre = jnp.dot(rows_in, w_gate, preferred_element_type=jnp.float32)
    up_pre = jnp.dot(rows_in, w_up, preferred_element_type=jnp.float32)
    sigmoid_gate = jax.nn.sigmoid(gate_pre)
    silu_gate = gate_pre * sigmoid_gate
    hidden = (silu_gate * up_pre).astype(jnp.bfloat16)
    hidden_grad = jnp.dot(grads_in, w_down, preferred_element_type=jnp.float32)
    gate_grad = (
        hidden_grad * up_pre * sigmoid_gate * (1.0 + gate_pre * (1.0 - sigmoid_gate))
    ).astype(jnp.bfloat16)
    up_grad = (hidden_grad * silu_gate).astype(jnp.bfloat16)
    contract_hidden = (((1,), (1,)), ((), ()))
    half = width // 2
    pieces = []
    for h in range(2):
        cols = slice(h * half, (h + 1) * half)
        row_grad = (
            lax.dot_general(gate_grad, w_gate[cols], contract_hidden, preferred_element_type=jnp.float32)
            + lax.dot_general(up_grad, w_up[cols], contract_hidden, preferred_element_type=jnp.float32)
        ).astype(jnp.bfloat16)
        back_rows = backward_move(row_grad.reshape(block[:-1] + (half,)), h == 0)
        pieces.append(
            lax.dot_general(
                picker,
                back_rows.reshape(positions, half),
                (((0,), (0,)), ((), ())),
                preferred_element_type=jnp.float32,
            ).astype(jnp.bfloat16)
        )
    token_grad = jnp.concatenate(pieces, 1)
    down_grad = lax.psum_scatter(
        lax.dot_general(
            grads_in, hidden, (((0,), (0,)), ((), ())), preferred_element_type=jnp.float32
        ).astype(jnp.bfloat16),
        "dp",
        scatter_dimension=0,
        tiled=True,
    )
    return (token_grad, down_grad[None])


def solution(mesh):
    n_dp, n_expert = mesh.devices.shape
    fine = Mesh(mesh.devices.reshape(n_dp, 2, n_expert // 4, 2), ("dp",) + SUB)
    rows = P(ROWS, None)
    weights = P(SUB, "dp", None)
    return jax.shard_map(
        body,
        mesh=fine,
        in_specs=(rows, rows, rows, rows, weights, weights, weights),
        out_specs=(rows, weights),
        check_vma=False,
    )
```

```python
import jax
import jax.numpy as jnp
from jax import lax
from jax.sharding import Mesh
from jax.sharding import PartitionSpec as P

TOP = 2
CAP = 5
SUB = ("ylo", "z", "core")
ROWS = ("dp",) + SUB
SWAP = [(0, 1), (1, 0)]


def swap_half(x, axis_name, dim):
    stay = lax.index_in_dim(x, 0, dim, keepdims=True)
    go = lax.index_in_dim(x, 1, dim, keepdims=True)
    got = lax.ppermute(go, axis_name, SWAP)
    return jnp.concatenate([stay, got], dim)


def forward_move(x, z_first):
    if z_first:
        x = lax.all_to_all(x, "z", 2, 2, tiled=True)
    x = swap_half(x, "core", 0)
    x = swap_half(x, "ylo", 1)
    if not z_first:
        x = lax.all_to_all(x, "z", 2, 2, tiled=True)
    return x


def backward_move(x, z_first):
    if z_first:
        x = lax.all_to_all(x, "z", 2, 2, tiled=True)
    x = swap_half(x, "ylo", 1)
    x = swap_half(x, "core", 0)
    if not z_first:
        x = lax.all_to_all(x, "z", 2, 2, tiled=True)
    return x


def body(tokens, out_grad, combine, expert_ids, gate_weight, up_weight, down_weight):
    token_rows = tokens.shape[0]
    width = tokens.shape[1]
    n_ylo, n_z, n_core = (lax.axis_size(a) for a in SUB)
    expert_count = n_ylo * n_z * n_core
    capacity = CAP
    positions = expert_count * capacity
    stacked = lax.all_gather(
        jnp.concatenate([gate_weight, up_weight, down_weight], 0), "dp", axis=1, tiled=True
    )
    w_gate, w_up, w_down = stacked[0], stacked[1], stacked[2]
    flat_ids = expert_ids.reshape(-1)
    onehot = (flat_ids[:, None] == jnp.arange(expert_count, dtype=jnp.int32)[None, :]).astype(jnp.int32)
    earlier = jnp.cumsum(onehot, axis=0) - onehot
    slot_index = jnp.sum(earlier * onehot, axis=1)
    my_core = lax.axis_index("core")
    my_ylo = lax.axis_index("ylo")
    e_core = flat_ids % n_core
    e_z = (flat_ids // n_core) % n_z
    e_ylo = flat_ids // (n_core * n_z)
    rel = ((e_core ^ my_core) * n_ylo + (e_ylo ^ my_ylo)) * n_z + e_z
    target = rel * capacity + slot_index
    matches = target[None, :] == jnp.arange(positions, dtype=jnp.int32)[:, None]
    picker = jnp.sum(
        matches.reshape(positions, token_rows, TOP).astype(jnp.float32), axis=2
    ).astype(jnp.bfloat16)
    slot_weight = jnp.sum(jnp.where(matches, combine.reshape(-1)[None, :], jnp.float32(0.0)), axis=1)
    row_send = jnp.dot(picker, tokens, preferred_element_type=jnp.float32).astype(jnp.bfloat16)
    picked_grad = jnp.dot(picker, out_grad, preferred_element_type=jnp.float32)
    grad_send = (slot_weight[:, None] * picked_grad).astype(jnp.bfloat16)
    block = (n_core, n_ylo, n_z, capacity, width)
    rows_in = forward_move(row_send.reshape(block), True).reshape(positions, width)
    grads_in = forward_move(grad_send.reshape(block), False).reshape(positions, width)
    gate_pre = jnp.dot(rows_in, w_gate, preferred_element_type=jnp.float32)
    up_pre = jnp.dot(rows_in, w_up, preferred_element_type=jnp.float32)
    sigmoid_gate = jax.nn.sigmoid(gate_pre)
    silu_gate = gate_pre * sigmoid_gate
    hidden = (silu_gate * up_pre).astype(jnp.bfloat16)
    hidden_grad = jnp.dot(grads_in, w_down, preferred_element_type=jnp.float32)
    gate_grad = (
        hidden_grad * up_pre * sigmoid_gate * (1.0 + gate_pre * (1.0 - sigmoid_gate))
    ).astype(jnp.bfloat16)
    up_grad = (hidden_grad * silu_gate).astype(jnp.bfloat16)
    contract_hidden = (((1,), (1,)), ((), ()))
    half = width // 2
    pieces = []
    for h in range(2):
        cols = slice(h * half, (h + 1) * half)
        row_grad = (
            lax.dot_general(gate_grad, w_gate[cols], contract_hidden, preferred_element_type=jnp.float32)
            + lax.dot_general(up_grad, w_up[cols], contract_hidden, preferred_element_type=jnp.float32)
        ).astype(jnp.bfloat16)
        back_rows = backward_move(row_grad.reshape(block[:-1] + (half,)), h == 0)
        pieces.append(
            lax.dot_general(
                picker,
                back_rows.reshape(positions, half),
                (((0,), (0,)), ((), ())),
                preferred_element_type=jnp.float32,
            ).astype(jnp.bfloat16)
        )
    token_grad = jnp.concatenate(pieces, 1)
    down_grad = lax.psum_scatter(
        lax.dot_general(
            grads_in, hidden, (((0,), (0,)), ((), ())), preferred_element_type=jnp.float32
        ).astype(jnp.bfloat16),
        "dp",
        scatter_dimension=0,
        tiled=True,
    )
    return (token_grad, down_grad[None])


def solution(mesh):
    n_dp, n_expert = mesh.devices.shape
    fine = Mesh(mesh.devices.reshape(n_dp, 2, n_expert // 4, 2), ("dp",) + SUB)
    rows = P(ROWS, None)
    weights = P(SUB, "dp", None)
    return jax.shard_map(
        body,
        mesh=fine,
        in_specs=(rows, rows, rows, rows, weights, weights, weights),
        out_specs=(rows, weights),
        check_vma=False,
    )
```

```python
import jax
import jax.numpy as jnp
from jax import lax
from jax.sharding import Mesh
from jax.sharding import PartitionSpec as P

TOP = 2
CAP = 5
SUB = ("ylo", "z", "core")
ROWS = ("dp",) + SUB
SWAP = [(0, 1), (1, 0)]


def swap_half(x, axis_name, dim):
    stay = lax.index_in_dim(x, 0, dim, keepdims=True)
    go = lax.index_in_dim(x, 1, dim, keepdims=True)
    got = lax.ppermute(go, axis_name, SWAP)
    return jnp.concatenate([stay, got], dim)


def forward_move(x, z_first):
    if z_first:
        x = lax.all_to_all(x, "z", 2, 2, tiled=True)
    x = swap_half(x, "core", 0)
    x = swap_half(x, "ylo", 1)
    if not z_first:
        x = lax.all_to_all(x, "z", 2, 2, tiled=True)
    return x


def backward_move(x, z_first):
    if z_first:
        x = lax.all_to_all(x, "z", 2, 2, tiled=True)
    x = swap_half(x, "ylo", 1)
    x = swap_half(x, "core", 0)
    if not z_first:
        x = lax.all_to_all(x, "z", 2, 2, tiled=True)
    return x


def body(tokens, out_grad, combine, expert_ids, gate_weight, up_weight, down_weight):
    token_rows = tokens.shape[0]
    width = tokens.shape[1]
    n_ylo, n_z, n_core = (lax.axis_size(a) for a in SUB)
    expert_count = n_ylo * n_z * n_core
    capacity = CAP
    positions = expert_count * capacity
    stacked = lax.all_gather(
        jnp.concatenate([gate_weight, up_weight, down_weight], 0), "dp", axis=1, tiled=True
    )
    w_gate, w_up, w_down = stacked[0], stacked[1], stacked[2]
    flat_ids = expert_ids.reshape(-1)
    onehot = (flat_ids[:, None] == jnp.arange(expert_count, dtype=jnp.int32)[None, :]).astype(jnp.int32)
    earlier = jnp.cumsum(onehot, axis=0) - onehot
    slot_index = jnp.sum(earlier * onehot, axis=1)
    my_core = lax.axis_index("core")
    my_ylo = lax.axis_index("ylo")
    e_core = flat_ids % n_core
    e_z = (flat_ids // n_core) % n_z
    e_ylo = flat_ids // (n_core * n_z)
    rel = ((e_core ^ my_core) * n_ylo + (e_ylo ^ my_ylo)) * n_z + e_z
    target = rel * capacity + slot_index
    matches = target[None, :] == jnp.arange(positions, dtype=jnp.int32)[:, None]
    picker = jnp.sum(
        matches.reshape(positions, token_rows, TOP).astype(jnp.float32), axis=2
    ).astype(jnp.bfloat16)
    slot_weight = jnp.sum(jnp.where(matches, combine.reshape(-1)[None, :], jnp.float32(0.0)), axis=1)
    row_send = jnp.dot(picker, tokens, preferred_element_type=jnp.float32).astype(jnp.bfloat16)
    picked_grad = jnp.dot(picker, out_grad, preferred_element_type=jnp.float32)
    grad_send = (slot_weight[:, None] * picked_grad).astype(jnp.bfloat16)
    block = (n_core, n_ylo, n_z * capacity, width)
    rows_in = forward_move(row_send.reshape(block), True).reshape(positions, width)
    grads_in = forward_move(grad_send.reshape(block), False).reshape(positions, width)
    gate_pre = jnp.dot(rows_in, w_gate, preferred_element_type=jnp.float32)
    up_pre = jnp.dot(rows_in, w_up, preferred_element_type=jnp.float32)
    sigmoid_gate = jax.nn.sigmoid(gate_pre)
    silu_gate = gate_pre * sigmoid_gate
    hidden = (silu_gate * up_pre).astype(jnp.bfloat16)
    hidden_grad = jnp.dot(grads_in, w_down, preferred_element_type=jnp.float32)
    gate_grad = (
        hidden_grad * up_pre * sigmoid_gate * (1.0 + gate_pre * (1.0 - sigmoid_gate))
    ).astype(jnp.bfloat16)
    up_grad = (hidden_grad * silu_gate).astype(jnp.bfloat16)
    contract_hidden = (((1,), (1,)), ((), ()))
    half = width // 2
    pieces = []
    for h in range(2):
        cols = slice(h * half, (h + 1) * half)
        row_grad = (
            lax.dot_general(gate_grad, w_gate[cols], contract_hidden, preferred_element_type=jnp.float32)
            + lax.dot_general(up_grad, w_up[cols], contract_hidden, preferred_element_type=jnp.float32)
        ).astype(jnp.bfloat16)
        back_rows = backward_move(row_grad.reshape(block[:-1] + (half,)), h == 0)
        pieces.append(
            lax.dot_general(
                picker,
                back_rows.reshape(positions, half),
                (((0,), (0,)), ((), ())),
                preferred_element_type=jnp.float32,
            ).astype(jnp.bfloat16)
        )
    token_grad = jnp.concatenate(pieces, 1)
    down_grad = lax.psum_scatter(
        lax.dot_general(
            grads_in, hidden, (((0,), (0,)), ((), ())), preferred_element_type=jnp.float32
        ).astype(jnp.bfloat16),
        "dp",
        scatter_dimension=0,
        tiled=True,
    )
    return (token_grad, down_grad[None])


def solution(mesh):
    n_dp, n_expert = mesh.devices.shape
    fine = Mesh(mesh.devices.reshape(n_dp, 2, n_expert // 4, 2), ("dp",) + SUB)
    rows = P(ROWS, None)
    weights = P(SUB, "dp", None)
    return jax.shard_map(
        body,
        mesh=fine,
        in_specs=(rows, rows, rows, rows, weights, weights, weights),
        out_specs=(rows, weights),
        check_vma=False,
    )
```

```python
import jax
import jax.numpy as jnp
from jax import lax
from jax.sharding import Mesh
from jax.sharding import PartitionSpec as P

TOP = 2
CAP = 5
SUB = ("ylo", "z", "core")
DP = ("x", "yhi")
ROWS = DP + SUB
SWAP = [(0, 1), (1, 0)]


def swap_half(x, axis_name, dim):
    stay = lax.index_in_dim(x, 0, dim, keepdims=True)
    go = lax.index_in_dim(x, 1, dim, keepdims=True)
    got = lax.ppermute(go, axis_name, SWAP)
    return jnp.concatenate([stay, got], dim)


def forward_move(x, z_first):
    if z_first:
        x = lax.all_to_all(x, "z", 2, 2, tiled=True)
    x = swap_half(x, "core", 0)
    x = swap_half(x, "ylo", 1)
    if not z_first:
        x = lax.all_to_all(x, "z", 2, 2, tiled=True)
    return x


def backward_move(x, z_first):
    if z_first:
        x = lax.all_to_all(x, "z", 2, 2, tiled=True)
    x = swap_half(x, "ylo", 1)
    x = swap_half(x, "core", 0)
    if not z_first:
        x = lax.all_to_all(x, "z", 2, 2, tiled=True)
    return x


def gather_weights(w):
    n_x = lax.axis_size("x")
    n_y = lax.axis_size("yhi")
    x_i = lax.axis_index("x")
    y_i = lax.axis_index("yhi")
    right = [(i, (i + 1) % n_x) for i in range(n_x)]
    left = [(i, (i - 1) % n_x) for i in range(n_x)]
    w_y = lax.ppermute(w, "yhi", SWAP)
    from_left = lax.ppermute(w, "x", right)
    from_right = lax.ppermute(w, "x", left)
    y_from_left = lax.ppermute(w_y, "x", right)
    y_from_right = lax.ppermute(w_y, "x", left)
    far = lax.ppermute(from_right, "x", left)
    y_far = lax.ppermute(y_from_left, "x", right)
    pieces = [
        (0, 0, w), (0, 1, w_y), (-1, 0, from_left), (1, 0, from_right),
        (-1, 1, y_from_left), (1, 1, y_from_right), (2, 0, far), (2, 1, y_far),
    ]
    rows = w.shape[1]
    full = jnp.zeros((w.shape[0], rows * n_x * n_y, w.shape[2]), w.dtype)
    for dx, dy, piece in pieces:
        owner = ((x_i + dx) % n_x) * n_y + (y_i ^ dy)
        full = lax.dynamic_update_slice(full, piece, (0, owner * rows, 0))
    return full


def body(tokens, out_grad, combine, expert_ids, gate_weight, up_weight, down_weight):
    token_rows = tokens.shape[0]
    width = tokens.shape[1]
    n_ylo, n_z, n_core = (lax.axis_size(a) for a in SUB)
    expert_count = n_ylo * n_z * n_core
    capacity = CAP
    positions = expert_count * capacity
    stacked = gather_weights(jnp.concatenate([gate_weight, up_weight, down_weight], 0))
    w_gate, w_up, w_down = stacked[0], stacked[1], stacked[2]
    flat_ids = expert_ids.reshape(-1)
    onehot = (flat_ids[:, None] == jnp.arange(expert_count, dtype=jnp.int32)[None, :]).astype(jnp.int32)
    earlier = jnp.cumsum(onehot, axis=0) - onehot
    slot_index = jnp.sum(earlier * onehot, axis=1)
    my_core = lax.axis_index("core")
    my_ylo = lax.axis_index("ylo")
    e_core = flat_ids % n_core
    e_z = (flat_ids // n_core) % n_z
    e_ylo = flat_ids // (n_core * n_z)
    rel = ((e_core ^ my_core) * n_ylo + (e_ylo ^ my_ylo)) * n_z + e_z
    target = rel * capacity + slot_index
    matches = target[None, :] == jnp.arange(positions, dtype=jnp.int32)[:, None]
    picker = jnp.sum(
        matches.reshape(positions, token_rows, TOP).astype(jnp.float32), axis=2
    ).astype(jnp.bfloat16)
    slot_weight = jnp.sum(jnp.where(matches, combine.reshape(-1)[None, :], jnp.float32(0.0)), axis=1)
    row_send = jnp.dot(picker, tokens, preferred_element_type=jnp.float32).astype(jnp.bfloat16)
    picked_grad = jnp.dot(picker, out_grad, preferred_element_type=jnp.float32)
    grad_send = (slot_weight[:, None] * picked_grad).astype(jnp.bfloat16)
    block = (n_core, n_ylo, n_z * capacity, width)
    rows_in = forward_move(row_send.reshape(block), True).reshape(positions, width)
    grads_in = forward_move(grad_send.reshape(block), False).reshape(positions, width)
    gate_pre = jnp.dot(rows_in, w_gate, preferred_element_type=jnp.float32)
    up_pre = jnp.dot(rows_in, w_up, preferred_element_type=jnp.float32)
    sigmoid_gate = jax.nn.sigmoid(gate_pre)
    silu_gate = gate_pre * sigmoid_gate
    hidden = (silu_gate * up_pre).astype(jnp.bfloat16)
    hidden_grad = jnp.dot(grads_in, w_down, preferred_element_type=jnp.float32)
    gate_grad = (
        hidden_grad * up_pre * sigmoid_gate * (1.0 + gate_pre * (1.0 - sigmoid_gate))
    ).astype(jnp.bfloat16)
    up_grad = (hidden_grad * silu_gate).astype(jnp.bfloat16)
    contract_hidden = (((1,), (1,)), ((), ()))
    half = width // 2
    pieces = []
    for h in range(2):
        cols = slice(h * half, (h + 1) * half)
        row_grad = (
            lax.dot_general(gate_grad, w_gate[cols], contract_hidden, preferred_element_type=jnp.float32)
            + lax.dot_general(up_grad, w_up[cols], contract_hidden, preferred_element_type=jnp.float32)
        ).astype(jnp.bfloat16)
        back_rows = backward_move(row_grad.reshape(block[:-1] + (half,)), h == 0)
        pieces.append(
            lax.dot_general(
                picker,
                back_rows.reshape(positions, half),
                (((0,), (0,)), ((), ())),
                preferred_element_type=jnp.float32,
            ).astype(jnp.bfloat16)
        )
    token_grad = jnp.concatenate(pieces, 1)
    down_grad = lax.psum_scatter(
        lax.dot_general(
            grads_in, hidden, (((0,), (0,)), ((), ())), preferred_element_type=jnp.float32
        ).astype(jnp.bfloat16),
        DP,
        scatter_dimension=0,
        tiled=True,
    )
    return (token_grad, down_grad[None])


def solution(mesh):
    n_dp, n_expert = mesh.devices.shape
    fine = Mesh(mesh.devices.reshape(n_dp // 2, 2, 2, n_expert // 4, 2), DP + SUB)
    rows = P(ROWS, None)
    weights = P(SUB, DP, None)
    return jax.shard_map(
        body,
        mesh=fine,
        in_specs=(rows, rows, rows, rows, weights, weights, weights),
        out_specs=(rows, weights),
        check_vma=False,
    )
```

```python
import jax
import jax.numpy as jnp
from jax import lax
from jax.sharding import Mesh
from jax.sharding import PartitionSpec as P

TOP = 2
CAP = 5
SUB = ("ylo", "z", "core")
DP = ("x", "yhi")
ROWS = DP + SUB
SWAP = [(0, 1), (1, 0)]


def swap_half(x, axis_name, dim):
    stay = lax.index_in_dim(x, 0, dim, keepdims=True)
    go = lax.index_in_dim(x, 1, dim, keepdims=True)
    got = lax.ppermute(go, axis_name, SWAP)
    return jnp.concatenate([stay, got], dim)


def forward_move(x, z_first):
    if z_first:
        x = lax.all_to_all(x, "z", 2, 2, tiled=True)
    x = swap_half(x, "core", 0)
    x = swap_half(x, "ylo", 1)
    if not z_first:
        x = lax.all_to_all(x, "z", 2, 2, tiled=True)
    return x


def backward_move(x, z_first):
    if z_first:
        x = lax.all_to_all(x, "z", 2, 2, tiled=True)
    x = swap_half(x, "ylo", 1)
    x = swap_half(x, "core", 0)
    if not z_first:
        x = lax.all_to_all(x, "z", 2, 2, tiled=True)
    return x


def gather_weights(w):
    n_x = lax.axis_size("x")
    n_y = lax.axis_size("yhi")
    x_i = lax.axis_index("x")
    y_i = lax.axis_index("yhi")
    right = [(i, (i + 1) % n_x) for i in range(n_x)]
    left = [(i, (i - 1) % n_x) for i in range(n_x)]
    w_y = lax.ppermute(w, "yhi", SWAP)
    from_left = lax.ppermute(w, "x", right)
    from_right = lax.ppermute(w, "x", left)
    y_from_left = lax.ppermute(w_y, "x", right)
    y_from_right = lax.ppermute(w_y, "x", left)
    far = lax.ppermute(from_right, "x", left)
    y_far = lax.ppermute(y_from_left, "x", right)
    pieces = [
        (0, 0, w), (0, 1, w_y), (-1, 0, from_left), (1, 0, from_right),
        (-1, 1, y_from_left), (1, 1, y_from_right), (2, 0, far), (2, 1, y_far),
    ]
    rows = w.shape[1]
    full = jnp.zeros((w.shape[0], rows * n_x * n_y, w.shape[2]), w.dtype)
    for dx, dy, piece in pieces:
        owner = ((x_i + dx) % n_x) * n_y + (y_i ^ dy)
        full = lax.dynamic_update_slice(full, piece, (0, owner * rows, 0))
    return full


def body(tokens, out_grad, combine, expert_ids, gate_weight, up_weight, down_weight):
    token_rows = tokens.shape[0]
    width = tokens.shape[1]
    n_ylo, n_z, n_core = (lax.axis_size(a) for a in SUB)
    expert_count = n_ylo * n_z * n_core
    capacity = CAP
    positions = expert_count * capacity
    stacked = lax.all_gather(jnp.concatenate([gate_weight, up_weight], 0), DP, axis=1, tiled=True)
    w_gate, w_up = stacked[0], stacked[1]
    w_down = gather_weights(down_weight)[0]
    flat_ids = expert_ids.reshape(-1)
    onehot = (flat_ids[:, None] == jnp.arange(expert_count, dtype=jnp.int32)[None, :]).astype(jnp.int32)
    earlier = jnp.cumsum(onehot, axis=0) - onehot
    slot_index = jnp.sum(earlier * onehot, axis=1)
    my_core = lax.axis_index("core")
    my_ylo = lax.axis_index("ylo")
    e_core = flat_ids % n_core
    e_z = (flat_ids // n_core) % n_z
    e_ylo = flat_ids // (n_core * n_z)
    rel = ((e_core ^ my_core) * n_ylo + (e_ylo ^ my_ylo)) * n_z + e_z
    target = rel * capacity + slot_index
    matches = target[None, :] == jnp.arange(positions, dtype=jnp.int32)[:, None]
    picker = jnp.sum(
        matches.reshape(positions, token_rows, TOP).astype(jnp.float32), axis=2
    ).astype(jnp.bfloat16)
    slot_weight = jnp.sum(jnp.where(matches, combine.reshape(-1)[None, :], jnp.float32(0.0)), axis=1)
    row_send = jnp.dot(picker, tokens, preferred_element_type=jnp.float32).astype(jnp.bfloat16)
    picked_grad = jnp.dot(picker, out_grad, preferred_element_type=jnp.float32)
    grad_send = (slot_weight[:, None] * picked_grad).astype(jnp.bfloat16)
    block = (n_core, n_ylo, n_z * capacity, width)
    rows_in = forward_move(row_send.reshape(block), True).reshape(positions, width)
    grads_in = forward_move(grad_send.reshape(block), False).reshape(positions, width)
    gate_pre = jnp.dot(rows_in, w_gate, preferred_element_type=jnp.float32)
    up_pre = jnp.dot(rows_in, w_up, preferred_element_type=jnp.float32)
    sigmoid_gate = jax.nn.sigmoid(gate_pre)
    silu_gate = gate_pre * sigmoid_gate
    hidden = (silu_gate * up_pre).astype(jnp.bfloat16)
    hidden_grad = jnp.dot(grads_in, w_down, preferred_element_type=jnp.float32)
    gate_grad = (
        hidden_grad * up_pre * sigmoid_gate * (1.0 + gate_pre * (1.0 - sigmoid_gate))
    ).astype(jnp.bfloat16)
    up_grad = (hidden_grad * silu_gate).astype(jnp.bfloat16)
    contract_hidden = (((1,), (1,)), ((), ()))
    half = width // 2
    pieces = []
    for h in range(2):
        cols = slice(h * half, (h + 1) * half)
        row_grad = (
            lax.dot_general(gate_grad, w_gate[cols], contract_hidden, preferred_element_type=jnp.float32)
            + lax.dot_general(up_grad, w_up[cols], contract_hidden, preferred_element_type=jnp.float32)
        ).astype(jnp.bfloat16)
        back_rows = backward_move(row_grad.reshape(block[:-1] + (half,)), h == 0)
        pieces.append(
            lax.dot_general(
                picker,
                back_rows.reshape(positions, half),
                (((0,), (0,)), ((), ())),
                preferred_element_type=jnp.float32,
            ).astype(jnp.bfloat16)
        )
    token_grad = jnp.concatenate(pieces, 1)
    down_grad = lax.psum_scatter(
        lax.dot_general(
            grads_in, hidden, (((0,), (0,)), ((), ())), preferred_element_type=jnp.float32
        ).astype(jnp.bfloat16),
        DP,
        scatter_dimension=0,
        tiled=True,
    )
    return (token_grad, down_grad[None])


def solution(mesh):
    n_dp, n_expert = mesh.devices.shape
    fine = Mesh(mesh.devices.reshape(n_dp // 2, 2, 2, n_expert // 4, 2), DP + SUB)
    rows = P(ROWS, None)
    weights = P(SUB, DP, None)
    return jax.shard_map(
        body,
        mesh=fine,
        in_specs=(rows, rows, rows, rows, weights, weights, weights),
        out_specs=(rows, weights),
        check_vma=False,
    )
```

```python
import jax
import jax.numpy as jnp
from jax import lax
from jax.sharding import Mesh
from jax.sharding import PartitionSpec as P

TOP = 2
CAP = 5
SUB = ("ylo", "z", "core")
DP = ("x", "yhi")
ROWS = DP + SUB
SWAP = [(0, 1), (1, 0)]


def swap_half(x, axis_name, dim):
    stay = lax.index_in_dim(x, 0, dim, keepdims=True)
    go = lax.index_in_dim(x, 1, dim, keepdims=True)
    got = lax.ppermute(go, axis_name, SWAP)
    return jnp.concatenate([stay, got], dim)


def forward_move(x, z_first):
    if z_first:
        x = lax.all_to_all(x, "z", 2, 2, tiled=True)
    x = swap_half(x, "core", 0)
    x = swap_half(x, "ylo", 1)
    if not z_first:
        x = lax.all_to_all(x, "z", 2, 2, tiled=True)
    return x


def backward_move(x, z_first):
    if z_first:
        x = lax.all_to_all(x, "z", 2, 2, tiled=True)
    x = swap_half(x, "ylo", 1)
    x = swap_half(x, "core", 0)
    if not z_first:
        x = lax.all_to_all(x, "z", 2, 2, tiled=True)
    return x


def gather_weights(w):
    n_x = lax.axis_size("x")
    n_y = lax.axis_size("yhi")
    x_i = lax.axis_index("x")
    y_i = lax.axis_index("yhi")
    right = [(i, (i + 1) % n_x) for i in range(n_x)]
    left = [(i, (i - 1) % n_x) for i in range(n_x)]
    w_y = lax.ppermute(w, "yhi", SWAP)
    from_left = lax.ppermute(w, "x", right)
    from_right = lax.ppermute(w, "x", left)
    y_from_left = lax.ppermute(w_y, "x", right)
    y_from_right = lax.ppermute(w_y, "x", left)
    far = lax.ppermute(from_right, "x", left)
    y_far = lax.ppermute(y_from_left, "x", right)
    pieces = [
        (0, 0, w), (0, 1, w_y), (-1, 0, from_left), (1, 0, from_right),
        (-1, 1, y_from_left), (1, 1, y_from_right), (2, 0, far), (2, 1, y_far),
    ]
    rows = w.shape[1]
    full = jnp.zeros((w.shape[0], rows * n_x * n_y, w.shape[2]), w.dtype)
    for dx, dy, piece in pieces:
        owner = ((x_i + dx) % n_x) * n_y + (y_i ^ dy)
        full = lax.dynamic_update_slice(full, piece, (0, owner * rows, 0))
    return full


def body(tokens, out_grad, combine, expert_ids, gate_weight, up_weight, down_weight):
    token_rows = tokens.shape[0]
    width = tokens.shape[1]
    n_ylo, n_z, n_core = (lax.axis_size(a) for a in SUB)
    expert_count = n_ylo * n_z * n_core
    capacity = CAP
    positions = expert_count * capacity
    stacked = lax.all_gather(jnp.concatenate([gate_weight, up_weight], 0), DP, axis=1, tiled=True)
    w_gate, w_up = stacked[0], stacked[1]
    w_down = gather_weights(down_weight)[0]
    flat_ids = expert_ids.reshape(-1)
    onehot = (flat_ids[:, None] == jnp.arange(expert_count, dtype=jnp.int32)[None, :]).astype(jnp.int32)
    earlier = jnp.cumsum(onehot, axis=0) - onehot
    slot_index = jnp.sum(earlier * onehot, axis=1)
    my_core = lax.axis_index("core")
    my_ylo = lax.axis_index("ylo")
    e_core = flat_ids % n_core
    e_z = (flat_ids // n_core) % n_z
    e_ylo = flat_ids // (n_core * n_z)
    rel = ((e_core ^ my_core) * n_ylo + (e_ylo ^ my_ylo)) * n_z + e_z
    target = rel * capacity + slot_index
    matches = target[None, :] == jnp.arange(positions, dtype=jnp.int32)[:, None]
    picker = jnp.sum(
        matches.reshape(positions, token_rows, TOP).astype(jnp.float32), axis=2
    ).astype(jnp.bfloat16)
    slot_weight = jnp.sum(jnp.where(matches, combine.reshape(-1)[None, :], jnp.float32(0.0)), axis=1)
    row_send = jnp.dot(picker, tokens, preferred_element_type=jnp.float32).astype(jnp.bfloat16)
    picked_grad = jnp.dot(picker, out_grad, preferred_element_type=jnp.float32)
    grad_send = (slot_weight[:, None] * picked_grad).astype(jnp.bfloat16)
    block = (n_core, n_ylo, n_z * capacity, width)
    rows_in = forward_move(row_send.reshape(block), True).reshape(positions, width)
    grads_in = forward_move(grad_send.reshape(block), False).reshape(positions, width)
    gate_pre = jnp.dot(rows_in, w_gate, preferred_element_type=jnp.float32)
    up_pre = jnp.dot(rows_in, w_up, preferred_element_type=jnp.float32)
    sigmoid_gate = jax.nn.sigmoid(gate_pre)
    silu_gate = gate_pre * sigmoid_gate
    hidden = (silu_gate * up_pre).astype(jnp.bfloat16)
    hidden_grad = jnp.dot(grads_in, w_down, preferred_element_type=jnp.float32)
    gate_grad = (
        hidden_grad * up_pre * sigmoid_gate * (1.0 + gate_pre * (1.0 - sigmoid_gate))
    ).astype(jnp.bfloat16)
    up_grad = (hidden_grad * silu_gate).astype(jnp.bfloat16)
    contract_hidden = (((1,), (1,)), ((), ()))
    half = width // 2
    pieces = []
    for h in range(2):
        cols = slice(h * half, (h + 1) * half)
        row_grad = (
            lax.dot_general(gate_grad, w_gate[cols], contract_hidden, preferred_element_type=jnp.float32)
            + lax.dot_general(up_grad, w_up[cols], contract_hidden, preferred_element_type=jnp.float32)
        ).astype(jnp.bfloat16)
        back_rows = backward_move(row_grad.reshape(block[:-1] + (half,)), h == 0)
        pieces.append(
            lax.dot_general(
                picker,
                back_rows.reshape(positions, half),
                (((0,), (0,)), ((), ())),
                preferred_element_type=jnp.float32,
            ).astype(jnp.bfloat16)
        )
    token_grad = jnp.concatenate(pieces, 1)
    down_term = lax.dot_general(
        grads_in, hidden, (((0,), (0,)), ((), ())), preferred_element_type=jnp.float32
    ).astype(jnp.bfloat16)
    n_x = lax.axis_size("x")
    y_i = lax.axis_index("yhi")
    blocks = down_term.reshape(n_x, 2, -1, down_term.shape[1])
    keep = lax.dynamic_index_in_dim(blocks, y_i, axis=1, keepdims=False)
    got = lax.ppermute(lax.dynamic_index_in_dim(blocks, 1 - y_i, axis=1, keepdims=False), "yhi", SWAP)
    pair = (keep.astype(jnp.float32) + got.astype(jnp.float32)).astype(jnp.bfloat16)
    down_grad = lax.psum_scatter(
        pair.reshape(-1, down_term.shape[1]), "x", scatter_dimension=0, tiled=True
    )
    return (token_grad, down_grad[None])


def solution(mesh):
    n_dp, n_expert = mesh.devices.shape
    fine = Mesh(mesh.devices.reshape(n_dp // 2, 2, 2, n_expert // 4, 2), DP + SUB)
    rows = P(ROWS, None)
    weights = P(SUB, DP, None)
    return jax.shard_map(
        body,
        mesh=fine,
        in_specs=(rows, rows, rows, rows, weights, weights, weights),
        out_specs=(rows, weights),
        check_vma=False,
    )
```
